32 devices in a mesh: row: 16 (over z, y, core), col: 2 (over x).
Axes of the slice: x: 2, y: 2, z: 4, core: 2. Of those that a mesh axis runs over, the one named last changes fastest.
Arguments:
- acts: bfloat16 [1024, 28672], P('row', 'col'), may hold values from -6 to 6
- grads: bfloat16 [1024, 8192], P('col', 'row'), may hold values from -6 to 6
- basis_in: bfloat16 [28672, 28672], P('row', 'col'), may hold values from -0.03125 to 0.03125
- basis_out: bfloat16 [8192, 8192], P('col', 'row'), may hold values from -0.0625 to 0.0625
- corr: float32 [28672, 8192], P('row', 'col'), may hold values from 0.5 to 2
Outputs:
- new_corr: float32 [28672, 8192], P('row', 'col')
The draws below stay inside these ranges and needn't reach their ends.
All inputs are finite; a program needn't handle non-finite values.
Results may differ from the reference program's by a relative error of at most 0.0026.
Values may be sent and summed in bfloat16 or wider, within the bound.
No kernel may reach another device: no remote copies, remote signals or barrier semaphores. Data moves between devices by JAX's collectives and lax.ppermute only.
A program may use at most 320 MiB of HBM per device.

```python
import jax
import jax.numpy as jnp
from jax import lax

IN = 28672
OUT = 8192
SEQ_LEN = 512
SEQS = 2
TOK = 1024
N_ROW = 16


def steps_of(own_key, dims, split, low, largest):
    gain = 1.0
    for position, blocks in split:
        steps = jax.random.uniform(jax.random.fold_in(jax.random.fold_in(own_key, 6), position), (blocks,), jnp.float32, low / len(split), largest / len(split))
        gain = gain * jnp.repeat(jnp.exp(steps), dims[position] // blocks).reshape((-1,) + (1,) * (len(dims) - 1 - position))
    return gain


def normal_values(rng, extent, spread, limit, shards=(), held_as=jnp.bfloat16):
    factor_of = steps_of(rng, extent, shards, -0.22, 0.18) if shards else 1.0
    result = jax.random.normal(rng, extent, jnp.float32) * spread * factor_of
    return jnp.minimum(jnp.maximum(result, -limit), limit).astype(held_as)


def setup_inputs(seed: int = 0) -> dict:
    key_of = jax.random.split(jax.random.key(seed), 6)
    return {
        "acts": normal_values(key_of[0], (TOK, IN), 1.0, 6.0, ((0, 16), (1, 2))),
        "grads": normal_values(key_of[1], (TOK, OUT), 1.0, 6.0, ((0, 2), (1, 16))),
        "basis_in": normal_values(key_of[2], (IN, IN), IN ** -0.5, 0.03125, ((0, 16), (1, 2))),
        "basis_out": normal_values(key_of[3], (OUT, OUT), OUT ** -0.5, 0.0625, ((0, 2), (1, 16))),
        "corr": jnp.clip(0.5 + 1.5 * jax.random.uniform(key_of[4], (IN, OUT), jnp.float32) ** steps_of(key_of[4], (IN, OUT), ((0, 16), (1, 2)), -0.2, 0.2), 0.5, 2.0),
    }


def reference(acts, grads, basis_in, basis_out, corr):
    blocks = basis_in.reshape(N_ROW, IN // N_ROW, IN)

    def rotate_block(block_rows):
        return lax.dot_general(acts, block_rows, (((1,), (1,)), ((), ())), preferred_element_type=jnp.float32).astype(jnp.bfloat16)

    rotated = lax.map(rotate_block, blocks)
    act_rot = jnp.transpose(rotated, (1, 0, 2)).reshape(TOK, IN)
    grad_rot = lax.dot_general(grads, basis_out, (((1,), (1,)), ((), ())), preferred_element_type=jnp.float32).astype(jnp.bfloat16)
    total = corr
    scale_factor = 1.0 / (SEQS * SEQ_LEN)
    for seq_index in range(SEQS):
        act_seq = act_rot[seq_index * SEQ_LEN:(seq_index + 1) * SEQ_LEN]
        grad_seq = grad_rot[seq_index * SEQ_LEN:(seq_index + 1) * SEQ_LEN]
        seq_grad = lax.dot_general(act_seq, grad_seq, (((0,), (0,)), ((), ())), preferred_element_type=jnp.float32)
        total = total + seq_grad * seq_grad * scale_factor
    return total
```

```python
import jax
import jax.numpy as jnp
import numpy as np
from jax import lax
from jax.sharding import Mesh
from jax.sharding import PartitionSpec as P

SEQ_LEN = 512
SEQS = 2
CHUNKS = 2
ROW = ("rchip", "core")


def swap_perm(n):
    return [(i, i ^ 1) for i in range(n)]


def local(acts, grads, basis_in, basis_out, corr):
    n_chip = lax.axis_size("rchip")
    n_row = n_chip * 2
    n_col = lax.axis_size("col")
    tok_dev = acts.shape[0]
    half = tok_dev // CHUNKS
    tokens = tok_dev * n_row

    act_t = []
    for c in range(CHUNKS):
        gathered = lax.all_gather(acts[c * half:(c + 1) * half], ROW, axis=0, tiled=True)
        part = lax.dot_general(
            basis_in, gathered, (((1,), (1,)), ((), ())), preferred_element_type=jnp.float32
        )
        if n_col == 2:
            other = lax.ppermute(part.astype(jnp.bfloat16), "col", swap_perm(2))
            act_t.append((part + other.astype(jnp.float32)).astype(jnp.bfloat16))
        else:
            act_t.append(lax.psum(part, "col").astype(jnp.bfloat16))

    g_all = lax.all_gather(grads, "col", axis=0, tiled=True)
    g_all = g_all.reshape(n_row, CHUNKS, half, g_all.shape[1]).transpose(1, 0, 2, 3)
    g_all = g_all.reshape(tokens, grads.shape[1])
    g_part = lax.dot_general(
        g_all, basis_out, (((1,), (1,)), ((), ())), preferred_element_type=jnp.float32
    )
    core = lax.axis_index("core")
    pair = tokens // 2
    keep = lax.dynamic_slice_in_dim(g_part, core * pair, pair, axis=0)
    send = lax.dynamic_slice_in_dim(g_part, (1 - core) * pair, pair, axis=0)
    summed = keep + lax.ppermute(send, "core", swap_perm(2))
    share = lax.psum_scatter(summed, "rchip", scatter_dimension=0, tiled=True)
    grad_rot = lax.all_gather(share.astype(jnp.bfloat16), ("core", "rchip"), axis=0, tiled=True)

    seg = n_row * half // SEQS
    a = jnp.concatenate(act_t, axis=1).reshape(basis_in.shape[0], CHUNKS, SEQS, seg)
    g = grad_rot.reshape(CHUNKS, SEQS, seg, grad_rot.shape[1])
    seq_grad = jnp.einsum("kcsu,csum->skm", a, g, preferred_element_type=jnp.float32)
    scale_factor = 1.0 / (SEQS * SEQ_LEN)
    return corr + jnp.sum(seq_grad * seq_grad, axis=0) * scale_factor


def solution(mesh):
    devices = np.asarray(mesh.devices)
    n_row, n_col = devices.shape
    inner = Mesh(devices.reshape(n_row // 2, 2, n_col), ("rchip", "core", "col"))
    return jax.shard_map(
        local,
        mesh=inner,
        in_specs=(
            P(ROW, "col"),
            P("col", ROW),
            P(ROW, "col"),
            P("col", ROW),
            P(ROW, "col"),
        ),
        out_specs=P(ROW, "col"),
        check_vma=False,
    )
```

```python
import functools

import jax
import jax.numpy as jnp
import numpy as np
from jax import lax
from jax.sharding import Mesh
from jax.sharding import PartitionSpec as P

SEQ_LEN = 512
SEQS = 2
CHUNKS = 2
ROW = ("rchip", "core")


def swap_perm(n):
    return [(i, i ^ 1) for i in range(n)]


def chip_ring(devices):
    n_chip = devices.shape[0] // 2
    coords = [getattr(devices[2 * i, 0], "coords", None) for i in range(n_chip)]
    if any(c is None for c in coords):
        return list(range(n_chip))
    coords = [tuple(c) for c in coords]
    vary = [d for d in range(len(coords[0])) if len({c[d] for c in coords}) > 1]
    if len(vary) == 1:
        return sorted(range(n_chip), key=lambda i: coords[i][vary[0]])
    if len(vary) != 2:
        return list(range(n_chip))
    a, b = vary
    if len({c[a] for c in coords}) != 2:
        a, b = b, a
    if len({c[a] for c in coords}) != 2:
        return list(range(n_chip))
    lo = min(c[a] for c in coords)
    first = sorted([i for i in range(n_chip) if coords[i][a] == lo], key=lambda i: coords[i][b])
    second = sorted([i for i in range(n_chip) if coords[i][a] != lo], key=lambda i: -coords[i][b])
    return first + second


def ring_reduce_scatter(x, ring, axis):
    n = len(ring)
    blk = x.shape[0] // n
    ring_arr = jnp.asarray(ring, jnp.int32)
    pos_arr = jnp.asarray(np.argsort(ring), jnp.int32)
    p = pos_arr[lax.axis_index(axis)]
    cols = x.shape[1] // 2
    right = [(ring[i], ring[(i + 1) % n]) for i in range(n)]
    left = [(ring[i], ring[(i - 1) % n]) for i in range(n)]

    def block(part, pos):
        return lax.dynamic_slice_in_dim(part, ring_arr[pos % n] * blk, blk, axis=0)

    xa, xb = x[:, :cols], x[:, cols:]
    buf_a = block(xa, p - 1 + n)
    buf_b = block(xb, p + 1)
    for s in range(1, n):
        buf_a = lax.ppermute(buf_a, axis, right) + block(xa, p - 1 - s + 2 * n)
        buf_b = lax.ppermute(buf_b, axis, left) + block(xb, p + 1 + s)
    return jnp.concatenate([buf_a, buf_b], axis=1)


def local(ring, acts, grads, basis_in, basis_out, corr):
    n_chip = lax.axis_size("rchip")
    n_row = n_chip * 2
    n_col = lax.axis_size("col")
    tok_dev = acts.shape[0]
    half = tok_dev // CHUNKS
    tokens = tok_dev * n_row

    act_t = []
    for c in range(CHUNKS):
        gathered = lax.all_gather(acts[c * half:(c + 1) * half], ROW, axis=0, tiled=True)
        part = lax.dot_general(
            basis_in, gathered, (((1,), (1,)), ((), ())), preferred_element_type=jnp.float32
        )
        if n_col == 2:
            other = lax.ppermute(part.astype(jnp.bfloat16), "col", swap_perm(2))
            act_t.append((part + other.astype(jnp.float32)).astype(jnp.bfloat16))
        else:
            act_t.append(lax.psum(part, "col").astype(jnp.bfloat16))

    g_all = lax.all_gather(grads, "col", axis=0, tiled=True)
    g_all = g_all.reshape(n_row, CHUNKS, half, g_all.shape[1]).transpose(1, 0, 2, 3)
    g_all = g_all.reshape(tokens, grads.shape[1])
    g_part = lax.dot_general(
        g_all, basis_out, (((1,), (1,)), ((), ())), preferred_element_type=jnp.float32
    )
    core = lax.axis_index("core")
    pair = tokens // 2
    keep = lax.dynamic_slice_in_dim(g_part, core * pair, pair, axis=0)
    send = lax.dynamic_slice_in_dim(g_part, (1 - core) * pair, pair, axis=0)
    summed = keep + lax.ppermute(send, "core", swap_perm(2))
    share = ring_reduce_scatter(summed, ring, "rchip")
    grad_rot = lax.all_gather(share.astype(jnp.bfloat16), ("core", "rchip"), axis=0, tiled=True)

    seg = n_row * half // SEQS
    a = jnp.concatenate(act_t, axis=1).reshape(basis_in.shape[0], CHUNKS, SEQS, seg)
    g = grad_rot.reshape(CHUNKS, SEQS, seg, grad_rot.shape[1])
    seq_grad = jnp.einsum("kcsu,csum->skm", a, g, preferred_element_type=jnp.float32)
    scale_factor = 1.0 / (SEQS * SEQ_LEN)
    return corr + jnp.sum(seq_grad * seq_grad, axis=0) * scale_factor


def solution(mesh):
    devices = np.asarray(mesh.devices)
    n_row, n_col = devices.shape
    inner = Mesh(devices.reshape(n_row // 2, 2, n_col), ("rchip", "core", "col"))
    ring = chip_ring(devices)
    return jax.shard_map(
        functools.partial(local, ring),
        mesh=inner,
        in_specs=(
            P(ROW, "col"),
            P("col", ROW),
            P(ROW, "col"),
            P("col", ROW),
            P(ROW, "col"),
        ),
        out_specs=P(ROW, "col"),
        check_vma=False,
    )
```

```python
import functools

import jax
import jax.numpy as jnp
import numpy as np
from jax import lax
from jax.experimental import pallas as pl
from jax.experimental.pallas import tpu as pltpu
from jax.sharding import Mesh
from jax.sharding import PartitionSpec as P

SEQ_LEN = 512
SEQS = 2
CHUNKS = 2
ROW = ("rchip", "core")


def swap_perm(n):
    return [(i, i ^ 1) for i in range(n)]


def chip_ring(devices):
    n_chip = devices.shape[0] // 2
    coords = [getattr(devices[2 * i, 0], "coords", None) for i in range(n_chip)]
    if any(c is None for c in coords):
        return list(range(n_chip))
    coords = [tuple(c) for c in coords]
    vary = [d for d in range(len(coords[0])) if len({c[d] for c in coords}) > 1]
    if len(vary) == 1:
        return sorted(range(n_chip), key=lambda i: coords[i][vary[0]])
    if len(vary) != 2:
        return list(range(n_chip))
    a, b = vary
    if len({c[a] for c in coords}) != 2:
        a, b = b, a
    if len({c[a] for c in coords}) != 2:
        return list(range(n_chip))
    lo = min(c[a] for c in coords)
    first = sorted([i for i in range(n_chip) if coords[i][a] == lo], key=lambda i: coords[i][b])
    second = sorted([i for i in range(n_chip) if coords[i][a] != lo], key=lambda i: -coords[i][b])
    return first + second


def ring_reduce_scatter(x, ring, axis):
    n = len(ring)
    blk = x.shape[0] // n
    ring_arr = jnp.asarray(ring, jnp.int32)
    pos_arr = jnp.asarray(np.argsort(ring), jnp.int32)
    p = pos_arr[lax.axis_index(axis)]
    cols = x.shape[1] // 2
    right = [(ring[i], ring[(i + 1) % n]) for i in range(n)]
    left = [(ring[i], ring[(i - 1) % n]) for i in range(n)]

    def block(part, pos):
        return lax.dynamic_slice_in_dim(part, ring_arr[pos % n] * blk, blk, axis=0)

    xa, xb = x[:, :cols], x[:, cols:]
    buf_a = block(xa, p - 1 + n)
    buf_b = block(xb, p + 1)
    for s in range(1, n):
        buf_a = lax.ppermute(buf_a, axis, right) + block(xa, p - 1 - s + 2 * n)
        buf_b = lax.ppermute(buf_b, axis, left) + block(xb, p + 1 + s)
    return jnp.concatenate([buf_a, buf_b], axis=1)


def correction_kernel(seg, at_ref, g_ref, corr_ref, out_ref):
    total = None
    for s in range(SEQS):
        cols = slice(s * seg, (s + 1) * seg)
        sg = jnp.dot(at_ref[:, cols], g_ref[cols, :], preferred_element_type=jnp.float32)
        total = sg * sg if total is None else total + sg * sg
    out_ref[...] = corr_ref[...] + total * (1.0 / (SEQS * SEQ_LEN))


def correction(at, g, corr, tm=256):
    k, t = at.shape
    m = g.shape[1]
    tm = min(tm, m)
    seg = t // SEQS
    return pl.pallas_call(
        functools.partial(correction_kernel, seg),
        out_shape=jax.ShapeDtypeStruct((k, m), jnp.float32),
        grid=(m // tm,),
        in_specs=[
            pl.BlockSpec((k, t), lambda j: (0, 0)),
            pl.BlockSpec((t, tm), lambda j: (0, j)),
            pl.BlockSpec((k, tm), lambda j: (0, j)),
        ],
        out_specs=pl.BlockSpec((k, tm), lambda j: (0, j)),
        compiler_params=pltpu.CompilerParams(vmem_limit_bytes=48 * 1024 * 1024),
        cost_estimate=pl.CostEstimate(
            flops=2 * k * t * m + 3 * k * m,
            transcendentals=0,
            bytes_accessed=2 * k * t + 2 * t * m + 8 * k * m,
        ),
    )(at, g, corr)


def local(ring, acts, grads, basis_in, basis_out, corr):
    n_chip = lax.axis_size("rchip")
    n_row = n_chip * 2
    n_col = lax.axis_size("col")
    tok_dev = acts.shape[0]
    half = tok_dev // CHUNKS
    tokens = tok_dev * n_row

    act_t = []
    for c in range(CHUNKS):
        gathered = lax.all_gather(acts[c * half:(c + 1) * half], ROW, axis=0, tiled=True)
        part = lax.dot_general(
            basis_in, gathered, (((1,), (1,)), ((), ())), preferred_element_type=jnp.float32
        )
        if n_col == 2:
            other = lax.ppermute(part.astype(jnp.bfloat16), "col", swap_perm(2))
            act_t.append((part + other.astype(jnp.float32)).astype(jnp.bfloat16))
        else:
            act_t.append(lax.psum(part, "col").astype(jnp.bfloat16))

    if n_col == 2:
        other = lax.ppermute(grads, "col", swap_perm(2))
        first = lax.axis_index("col") == 0
        g_all = jnp.concatenate([jnp.where(first, grads, other), jnp.where(first, other, grads)])
    else:
        g_all = lax.all_gather(grads, "col", axis=0, tiled=True)
    per_seq = n_row // SEQS
    g_all = g_all.reshape(SEQS, per_seq, CHUNKS, half, g_all.shape[1]).transpose(0, 2, 1, 3, 4)
    g_all = g_all.reshape(tokens, grads.shape[1])
    g_part = lax.dot_general(
        g_all, basis_out, (((1,), (1,)), ((), ())), preferred_element_type=jnp.float32
    )
    core = lax.axis_index("core")
    pair = tokens // 2
    keep = lax.dynamic_slice_in_dim(g_part, core * pair, pair, axis=0)
    send = lax.dynamic_slice_in_dim(g_part, (1 - core) * pair, pair, axis=0)
    summed = keep + lax.ppermute(send, "core", swap_perm(2))
    share = ring_reduce_scatter(summed, ring, "rchip")
    grad_rot = lax.all_gather(share.astype(jnp.bfloat16), ("core", "rchip"), axis=0, tiled=True)

    seg = per_seq * half
    at = jnp.concatenate(
        [act_t[c][:, s * seg:(s + 1) * seg] for s in range(SEQS) for c in range(CHUNKS)], axis=1
    )
    return correction(at, grad_rot, corr)


def solution(mesh):
    devices = np.asarray(mesh.devices)
    n_row, n_col = devices.shape
    inner = Mesh(devices.reshape(n_row // 2, 2, n_col), ("rchip", "core", "col"))
    ring = chip_ring(devices)
    return jax.shard_map(
        functools.partial(local, ring),
        mesh=inner,
        in_specs=(
            P(ROW, "col"),
            P("col", ROW),
            P(ROW, "col"),
            P("col", ROW),
            P(ROW, "col"),
        ),
        out_specs=P(ROW, "col"),
        check_vma=False,
    )
```

```python
import functools

import jax
import jax.numpy as jnp
import numpy as np
from jax import lax
from jax.experimental import pallas as pl
from jax.experimental.pallas import tpu as pltpu
from jax.sharding import Mesh
from jax.sharding import PartitionSpec as P

SEQ_LEN = 512
SEQS = 2
CHUNKS = 2
ROW = ("rchip", "core")


def swap_perm(n):
    return [(i, i ^ 1) for i in range(n)]


def chip_ring(devices):
    n_chip = devices.shape[0] // 2
    coords = [getattr(devices[2 * i, 0], "coords", None) for i in range(n_chip)]
    if any(c is None for c in coords):
        return list(range(n_chip))
    coords = [tuple(c) for c in coords]
    vary = [d for d in range(len(coords[0])) if len({c[d] for c in coords}) > 1]
    if len(vary) == 1:
        return sorted(range(n_chip), key=lambda i: coords[i][vary[0]])
    if len(vary) != 2:
        return list(range(n_chip))
    a, b = vary
    if len({c[a] for c in coords}) != 2:
        a, b = b, a
    if len({c[a] for c in coords}) != 2:
        return list(range(n_chip))
    lo = min(c[a] for c in coords)
    first = sorted([i for i in range(n_chip) if coords[i][a] == lo], key=lambda i: coords[i][b])
    second = sorted([i for i in range(n_chip) if coords[i][a] != lo], key=lambda i: -coords[i][b])
    return first + second


def ring_reduce_scatter(x, ring, axis):
    n = len(ring)
    blk = x.shape[0] // n
    ring_arr = jnp.asarray(ring, jnp.int32)
    pos_arr = jnp.asarray(np.argsort(ring), jnp.int32)
    p = pos_arr[lax.axis_index(axis)]
    cols = x.shape[1] // 2
    right = [(ring[i], ring[(i + 1) % n]) for i in range(n)]
    left = [(ring[i], ring[(i - 1) % n]) for i in range(n)]

    def block(part, pos):
        return lax.dynamic_slice_in_dim(part, ring_arr[pos % n] * blk, blk, axis=0)

    xa, xb = x[:, :cols], x[:, cols:]
    buf_a = block(xa, p - 1 + n)
    buf_b = block(xb, p + 1)
    for s in range(1, n):
        buf_a = lax.ppermute(buf_a, axis, right) + block(xa, p - 1 - s + 2 * n)
        buf_b = lax.ppermute(buf_b, axis, left) + block(xb, p + 1 + s)
    return jnp.concatenate([buf_a, buf_b], axis=1)


def correction_kernel(a0_ref, a1_ref, g0_ref, g1_ref, corr_ref, out_ref):
    s0 = jnp.dot(a0_ref[...], g0_ref[...], preferred_element_type=jnp.float32)
    s1 = jnp.dot(a1_ref[...], g1_ref[...], preferred_element_type=jnp.float32)
    out_ref[...] = corr_ref[...] + (s0 * s0 + s1 * s1) * (1.0 / (SEQS * SEQ_LEN))


def correction(a0, a1, g0, g1, corr, tm=256):
    k, t = a0.shape
    m = g0.shape[1]
    tm = min(tm, m)
    a_spec = pl.BlockSpec((k, t), lambda j: (0, 0))
    g_spec = pl.BlockSpec((t, tm), lambda j: (0, j))
    c_spec = pl.BlockSpec((k, tm), lambda j: (0, j))
    return pl.pallas_call(
        correction_kernel,
        out_shape=jax.ShapeDtypeStruct((k, m), jnp.float32),
        grid=(m // tm,),
        in_specs=[a_spec, a_spec, g_spec, g_spec, c_spec],
        out_specs=c_spec,
        compiler_params=pltpu.CompilerParams(vmem_limit_bytes=48 * 1024 * 1024),
        cost_estimate=pl.CostEstimate(
            flops=4 * k * t * m + 4 * k * m,
            transcendentals=0,
            bytes_accessed=4 * k * t + 4 * t * m + 8 * k * m,
        ),
    )(a0, a1, g0, g1, corr)


def in_core_order(core, own, other, axis):
    first = core == 0
    return jnp.where(
        first,
        jnp.concatenate([own, other], axis=axis),
        jnp.concatenate([other, own], axis=axis),
    )


def local(ring, acts, grads, basis_in, basis_out, corr):
    assert SEQS == 2
    n_chip = lax.axis_size("rchip")
    n_row = n_chip * 2
    n_col = lax.axis_size("col")
    tok_dev = acts.shape[0]
    half = tok_dev // CHUNKS
    tokens = tok_dev * n_row
    k_rows = basis_in.shape[0]
    core = lax.axis_index("core")
    chip_seq = n_chip // SEQS
    seg = chip_seq * half

    act_t = []
    for c in range(CHUNKS):
        own = lax.all_gather(acts[c * half:(c + 1) * half], "rchip", axis=0, tiled=True)
        other = lax.ppermute(own, "core", swap_perm(2))
        dims = (((1,), (1,)), ((), ()))
        p_own = lax.dot_general(basis_in, own, dims, preferred_element_type=jnp.float32)
        p_other = lax.dot_general(basis_in, other, dims, preferred_element_type=jnp.float32)
        part = in_core_order(core, p_own, p_other, 1)
        if n_col == 2:
            swapped = lax.ppermute(part.astype(jnp.bfloat16), "col", swap_perm(2))
            act_t.append((part + swapped.astype(jnp.float32)).astype(jnp.bfloat16))
        else:
            act_t.append(lax.psum(part, "col").astype(jnp.bfloat16))
    a_seq = [
        jnp.concatenate(
            [x.reshape(k_rows, 2, SEQS, seg)[:, :, s, :].reshape(k_rows, 2 * seg) for x in act_t],
            axis=1,
        )
        for s in range(SEQS)
    ]

    if n_col == 2:
        peer = lax.ppermute(grads, "col", swap_perm(2))
        first = lax.axis_index("col") == 0
        g_all = jnp.concatenate([jnp.where(first, grads, peer), jnp.where(first, peer, grads)])
    else:
        g_all = lax.all_gather(grads, "col", axis=0, tiled=True)
    o_cols = grads.shape[1]
    g_all = g_all.reshape(SEQS, chip_seq, 2, CHUNKS, half, o_cols).transpose(0, 3, 2, 1, 4, 5)
    g_all = g_all.reshape(tokens, o_cols)
    g_part = lax.dot_general(
        g_all, basis_out, (((1,), (1,)), ((), ())), preferred_element_type=jnp.float32
    )
    pair = tokens // 2
    keep = lax.dynamic_slice_in_dim(g_part, core * pair, pair, axis=0)
    send = lax.dynamic_slice_in_dim(g_part, (1 - core) * pair, pair, axis=0)
    summed = keep + lax.ppermute(send, "core", swap_perm(2))
    share = ring_reduce_scatter(summed, ring, "rchip")
    g_own = lax.all_gather(share.astype(jnp.bfloat16), "rchip", axis=0, tiled=True)
    g_other = lax.ppermute(g_own, "core", swap_perm(2))
    a_own = jnp.where(core == 0, a_seq[0], a_seq[1])
    a_other = jnp.where(core == 0, a_seq[1], a_seq[0])
    return correction(a_own, a_other, g_own, g_other, corr)


def solution(mesh):
    devices = np.asarray(mesh.devices)
    n_row, n_col = devices.shape
    inner = Mesh(devices.reshape(n_row // 2, 2, n_col), ("rchip", "core", "col"))
    ring = chip_ring(devices)
    return jax.shard_map(
        functools.partial(local, ring),
        mesh=inner,
        in_specs=(
            P(ROW, "col"),
            P("col", ROW),
            P(ROW, "col"),
            P("col", ROW),
            P(ROW, "col"),
        ),
        out_specs=P(ROW, "col"),
        check_vma=False,
    )
```

```python
import functools

import jax
import jax.numpy as jnp
import numpy as np
from jax import lax
from jax.experimental import pallas as pl
from jax.experimental.pallas import tpu as pltpu
from jax.sharding import Mesh
from jax.sharding import PartitionSpec as P

SEQ_LEN = 512
SEQS = 2
CHUNKS = 1
ROW = ("rchip", "core")


def swap_perm(n):
    return [(i, i ^ 1) for i in range(n)]


def chip_ring(devices):
    n_chip = devices.shape[0] // 2
    coords = [getattr(devices[2 * i, 0], "coords", None) for i in range(n_chip)]
    if any(c is None for c in coords):
        return list(range(n_chip))
    coords = [tuple(c) for c in coords]
    vary = [d for d in range(len(coords[0])) if len({c[d] for c in coords}) > 1]
    if len(vary) == 1:
        return sorted(range(n_chip), key=lambda i: coords[i][vary[0]])
    if len(vary) != 2:
        return list(range(n_chip))
    a, b = vary
    if len({c[a] for c in coords}) != 2:
        a, b = b, a
    if len({c[a] for c in coords}) != 2:
        return list(range(n_chip))
    lo = min(c[a] for c in coords)
    first = sorted([i for i in range(n_chip) if coords[i][a] == lo], key=lambda i: coords[i][b])
    second = sorted([i for i in range(n_chip) if coords[i][a] != lo], key=lambda i: -coords[i][b])
    return first + second


def ring_reduce_scatter(x, ring, axis):
    n = len(ring)
    blk = x.shape[0] // n
    ring_arr = jnp.asarray(ring, jnp.int32)
    pos_arr = jnp.asarray(np.argsort(ring), jnp.int32)
    p = pos_arr[lax.axis_index(axis)]
    cols = x.shape[1] // 2
    right = [(ring[i], ring[(i + 1) % n]) for i in range(n)]
    left = [(ring[i], ring[(i - 1) % n]) for i in range(n)]

    def block(part, pos):
        return lax.dynamic_slice_in_dim(part, ring_arr[pos % n] * blk, blk, axis=0)

    xa, xb = x[:, :cols], x[:, cols:]
    buf_a = block(xa, p - 1 + n)
    buf_b = block(xb, p + 1)
    for s in range(1, n):
        buf_a = lax.ppermute(buf_a, axis, right) + block(xa, p - 1 - s + 2 * n)
        buf_b = lax.ppermute(buf_b, axis, left) + block(xb, p + 1 + s)
    return jnp.concatenate([buf_a, buf_b], axis=1)


def correction_kernel(seg, at_ref, g_ref, corr_ref, out_ref):
    total = None
    for s in range(SEQS):
        cols = slice(s * seg, (s + 1) * seg)
        sg = jnp.dot(at_ref[:, cols], g_ref[cols, :], preferred_element_type=jnp.float32)
        total = sg * sg if total is None else total + sg * sg
    out_ref[...] = corr_ref[...] + total * (1.0 / (SEQS * SEQ_LEN))


def correction(at, g, corr, tm=256):
    k, t = at.shape
    m = g.shape[1]
    tm = min(tm, m)
    seg = t // SEQS
    return pl.pallas_call(
        functools.partial(correction_kernel, seg),
        out_shape=jax.ShapeDtypeStruct((k, m), jnp.float32),
        grid=(m // tm,),
        in_specs=[
            pl.BlockSpec((k, t), lambda j: (0, 0)),
            pl.BlockSpec((t, tm), lambda j: (0, j)),
            pl.BlockSpec((k, tm), lambda j: (0, j)),
        ],
        out_specs=pl.BlockSpec((k, tm), lambda j: (0, j)),
        compiler_params=pltpu.CompilerParams(vmem_limit_bytes=48 * 1024 * 1024),
        cost_estimate=pl.CostEstimate(
            flops=2 * k * t * m + 3 * k * m,
            transcendentals=0,
            bytes_accessed=2 * k * t + 2 * t * m + 8 * k * m,
        ),
    )(at, g, corr)


def local(ring, acts, grads, basis_in, basis_out, corr):
    n_chip = lax.axis_size("rchip")
    n_row = n_chip * 2
    n_col = lax.axis_size("col")
    tok_dev = acts.shape[0]
    half = tok_dev // CHUNKS
    tokens = tok_dev * n_row

    act_t = []
    for c in range(CHUNKS):
        gathered = lax.all_gather(acts[c * half:(c + 1) * half], ROW, axis=0, tiled=True)
        part = lax.dot_general(
            basis_in, gathered, (((1,), (1,)), ((), ())), preferred_element_type=jnp.float32
        )
        if n_col == 2:
            other = lax.ppermute(part.astype(jnp.bfloat16), "col", swap_perm(2))
            act_t.append((part + other.astype(jnp.float32)).astype(jnp.bfloat16))
        else:
            act_t.append(lax.psum(part, "col").astype(jnp.bfloat16))

    if n_col == 2:
        other = lax.ppermute(grads, "col", swap_perm(2))
        first = lax.axis_index("col") == 0
        g_all = jnp.concatenate([jnp.where(first, grads, other), jnp.where(first, other, grads)])
    else:
        g_all = lax.all_gather(grads, "col", axis=0, tiled=True)
    per_seq = n_row // SEQS
    g_all = g_all.reshape(SEQS, per_seq, CHUNKS, half, g_all.shape[1]).transpose(0, 2, 1, 3, 4)
    g_all = g_all.reshape(tokens, grads.shape[1])
    g_part = lax.dot_general(
        g_all, basis_out, (((1,), (1,)), ((), ())), preferred_element_type=jnp.float32
    )
    core = lax.axis_index("core")
    pair = tokens // 2
    keep = lax.dynamic_slice_in_dim(g_part, core * pair, pair, axis=0)
    send = lax.dynamic_slice_in_dim(g_part, (1 - core) * pair, pair, axis=0)
    summed = keep + lax.ppermute(send, "core", swap_perm(2))
    share = ring_reduce_scatter(summed, ring, "rchip")
    grad_rot = lax.all_gather(share.astype(jnp.bfloat16), ("core", "rchip"), axis=0, tiled=True)

    seg = per_seq * half
    at = jnp.concatenate(
        [act_t[c][:, s * seg:(s + 1) * seg] for s in range(SEQS) for c in range(CHUNKS)], axis=1
    )
    return correction(at, grad_rot, corr)


def solution(mesh):
    devices = np.asarray(mesh.devices)
    n_row, n_col = devices.shape
    inner = Mesh(devices.reshape(n_row // 2, 2, n_col), ("rchip", "core", "col"))
    ring = chip_ring(devices)
    return jax.shard_map(
        functools.partial(local, ring),
        mesh=inner,
        in_specs=(
            P(ROW, "col"),
            P("col", ROW),
            P(ROW, "col"),
            P("col", ROW),
            P(ROW, "col"),
        ),
        out_specs=P(ROW, "col"),
        check_vma=False,
    )
```

```python
import functools

import jax
import jax.numpy as jnp
import numpy as np
from jax import lax
from jax.experimental import pallas as pl
from jax.experimental.pallas import tpu as pltpu
from jax.sharding import Mesh
from jax.sharding import PartitionSpec as P

SEQ_LEN = 512
SEQS = 2
CHUNKS = 1
K_PIECES = 2
ROW = ("rchip", "core")


def swap_perm(n):
    return [(i, i ^ 1) for i in range(n)]


def chip_ring(devices):
    n_chip = devices.shape[0] // 2
    coords = [getattr(devices[2 * i, 0], "coords", None) for i in range(n_chip)]
    if any(c is None for c in coords):
        return list(range(n_chip))
    coords = [tuple(c) for c in coords]
    vary = [d for d in range(len(coords[0])) if len({c[d] for c in coords}) > 1]
    if len(vary) == 1:
        return sorted(range(n_chip), key=lambda i: coords[i][vary[0]])
    if len(vary) != 2:
        return list(range(n_chip))
    a, b = vary
    if len({c[a] for c in coords}) != 2:
        a, b = b, a
    if len({c[a] for c in coords}) != 2:
        return list(range(n_chip))
    lo = min(c[a] for c in coords)
    first = sorted([i for i in range(n_chip) if coords[i][a] == lo], key=lambda i: coords[i][b])
    second = sorted([i for i in range(n_chip) if coords[i][a] != lo], key=lambda i: -coords[i][b])
    return first + second


def ring_reduce_scatter(x, ring, axis):
    n = len(ring)
    blk = x.shape[0] // n
    ring_arr = jnp.asarray(ring, jnp.int32)
    pos_arr = jnp.asarray(np.argsort(ring), jnp.int32)
    p = pos_arr[lax.axis_index(axis)]
    cols = x.shape[1] // 2
    right = [(ring[i], ring[(i + 1) % n]) for i in range(n)]
    left = [(ring[i], ring[(i - 1) % n]) for i in range(n)]

    def block(part, pos):
        return lax.dynamic_slice_in_dim(part, ring_arr[pos % n] * blk, blk, axis=0)

    xa, xb = x[:, :cols], x[:, cols:]
    buf_a = block(xa, p - 1 + n)
    buf_b = block(xb, p + 1)
    for s in range(1, n):
        buf_a = lax.ppermute(buf_a, axis, right) + block(xa, p - 1 - s + 2 * n)
        buf_b = lax.ppermute(buf_b, axis, left) + block(xb, p + 1 + s)
    return jnp.concatenate([buf_a, buf_b], axis=1)


def correction_kernel(seg, at_ref, g_ref, corr_ref, *rest):
    out_ref = rest[-1]
    total = None
    for s in range(SEQS):
        cols = slice(s * seg, (s + 1) * seg)
        sg = jnp.dot(at_ref[:, cols], g_ref[cols, :], preferred_element_type=jnp.float32)
        total = sg * sg if total is None else total + sg * sg
    out_ref[...] = corr_ref[...] + total * (1.0 / (SEQS * SEQ_LEN))


def correction(at, g, corr, piece, prev=None, tm=256):
    kp, t = at.shape
    m = g.shape[1]
    tm = min(tm, m)
    seg = t // SEQS
    in_specs = [
        pl.BlockSpec((kp, t), lambda j: (0, 0)),
        pl.BlockSpec((t, tm), lambda j: (0, j)),
        pl.BlockSpec((kp, tm), lambda j: (piece, j)),
    ]
    args = [at, g, corr]
    aliases = {}
    if prev is not None:
        in_specs.append(pl.BlockSpec(memory_space=pl.ANY))
        args.append(prev)
        aliases = {3: 0}
    return pl.pallas_call(
        functools.partial(correction_kernel, seg),
        out_shape=jax.ShapeDtypeStruct(corr.shape, jnp.float32),
        grid=(m // tm,),
        in_specs=in_specs,
        out_specs=pl.BlockSpec((kp, tm), lambda j: (piece, j)),
        input_output_aliases=aliases,
        compiler_params=pltpu.CompilerParams(vmem_limit_bytes=48 * 1024 * 1024),
        cost_estimate=pl.CostEstimate(
            flops=2 * kp * t * m + 3 * kp * m,
            transcendentals=0,
            bytes_accessed=2 * kp * t + 2 * t * m + 8 * kp * m,
        ),
    )(*args)


def local(ring, acts, grads, basis_in, basis_out, corr):
    n_chip = lax.axis_size("rchip")
    n_row = n_chip * 2
    n_col = lax.axis_size("col")
    tok_dev = acts.shape[0]
    assert CHUNKS == 1
    half = tok_dev // CHUNKS
    tokens = tok_dev * n_row

    gathered = lax.all_gather(acts, ROW, axis=0, tiled=True)
    k_rows = basis_in.shape[0]
    kp = k_rows // K_PIECES
    act_t = []
    for i in range(K_PIECES):
        part = lax.dot_general(
            basis_in[i * kp:(i + 1) * kp], gathered, (((1,), (1,)), ((), ())),
            preferred_element_type=jnp.float32,
        )
        if n_col == 2:
            other = lax.ppermute(part.astype(jnp.bfloat16), "col", swap_perm(2))
            act_t.append((part + other.astype(jnp.float32)).astype(jnp.bfloat16))
        else:
            act_t.append(lax.psum(part, "col").astype(jnp.bfloat16))

    if n_col == 2:
        other = lax.ppermute(grads, "col", swap_perm(2))
        first = lax.axis_index("col") == 0
        g_all = jnp.concatenate([jnp.where(first, grads, other), jnp.where(first, other, grads)])
    else:
        g_all = lax.all_gather(grads, "col", axis=0, tiled=True)
    per_seq = n_row // SEQS
    g_all = g_all.reshape(SEQS, per_seq, CHUNKS, half, g_all.shape[1]).transpose(0, 2, 1, 3, 4)
    g_all = g_all.reshape(tokens, grads.shape[1])
    g_part = lax.dot_general(
        g_all, basis_out, (((1,), (1,)), ((), ())), preferred_element_type=jnp.float32
    )
    core = lax.axis_index("core")
    pair = tokens // 2
    keep = lax.dynamic_slice_in_dim(g_part, core * pair, pair, axis=0)
    send = lax.dynamic_slice_in_dim(g_part, (1 - core) * pair, pair, axis=0)
    summed = keep + lax.ppermute(send, "core", swap_perm(2))
    share = ring_reduce_scatter(summed, ring, "rchip")
    grad_rot = lax.all_gather(share.astype(jnp.bfloat16), ("core", "rchip"), axis=0, tiled=True)

    out = None
    for i in range(K_PIECES):
        out = correction(act_t[i], grad_rot, corr, i, out)
    return out


def solution(mesh):
    devices = np.asarray(mesh.devices)
    n_row, n_col = devices.shape
    inner = Mesh(devices.reshape(n_row // 2, 2, n_col), ("rchip", "core", "col"))
    ring = chip_ring(devices)
    return jax.shard_map(
        functools.partial(local, ring),
        mesh=inner,
        in_specs=(
            P(ROW, "col"),
            P("col", ROW),
            P(ROW, "col"),
            P("col", ROW),
            P(ROW, "col"),
        ),
        out_specs=P(ROW, "col"),
        check_vma=False,
    )
```

```python
import functools

import jax
import jax.numpy as jnp
import numpy as np
from jax import lax
from jax.experimental import pallas as pl
from jax.experimental.pallas import tpu as pltpu
from jax.sharding import Mesh
from jax.sharding import PartitionSpec as P

SEQ_LEN = 512
SEQS = 2
CHUNKS = 1
K_PIECES = 2
ROW = ("rchip", "core")


def swap_perm(n):
    return [(i, i ^ 1) for i in range(n)]


def chip_ring(devices):
    n_chip = devices.shape[0] // 2
    coords = [getattr(devices[2 * i, 0], "coords", None) for i in range(n_chip)]
    if any(c is None for c in coords):
        return list(range(n_chip))
    coords = [tuple(c) for c in coords]
    vary = [d for d in range(len(coords[0])) if len({c[d] for c in coords}) > 1]
    if len(vary) == 1:
        return sorted(range(n_chip), key=lambda i: coords[i][vary[0]])
    if len(vary) != 2:
        return list(range(n_chip))
    a, b = vary
    if len({c[a] for c in coords}) != 2:
        a, b = b, a
    if len({c[a] for c in coords}) != 2:
        return list(range(n_chip))
    lo = min(c[a] for c in coords)
    first = sorted([i for i in range(n_chip) if coords[i][a] == lo], key=lambda i: coords[i][b])
    second = sorted([i for i in range(n_chip) if coords[i][a] != lo], key=lambda i: -coords[i][b])
    return first + second


def ring_reduce_scatter(x, ring, axis):
    n = len(ring)
    blk = x.shape[0] // n
    ring_arr = jnp.asarray(ring, jnp.int32)
    pos_arr = jnp.asarray(np.argsort(ring), jnp.int32)
    p = pos_arr[lax.axis_index(axis)]
    cols = x.shape[1] // 2
    right = [(ring[i], ring[(i + 1) % n]) for i in range(n)]
    left = [(ring[i], ring[(i - 1) % n]) for i in range(n)]

    def block(part, pos):
        return lax.dynamic_slice_in_dim(part, ring_arr[pos % n] * blk, blk, axis=0)

    xa, xb = x[:, :cols], x[:, cols:]
    buf_a = block(xa, p - 1 + n)
    buf_b = block(xb, p + 1)
    for s in range(1, n):
        buf_a = lax.ppermute(buf_a, axis, right) + block(xa, p - 1 - s + 2 * n)
        buf_b = lax.ppermute(buf_b, axis, left) + block(xb, p + 1 + s)
    return jnp.concatenate([buf_a, buf_b], axis=1)


def correction_kernel(seg, at_ref, g_ref, corr_ref, *rest):
    out_ref = rest[-1]
    total = None
    for s in range(SEQS):
        cols = slice(s * seg, (s + 1) * seg)
        sg = jnp.dot(at_ref[:, cols], g_ref[cols, :], preferred_element_type=jnp.float32)
        total = sg * sg if total is None else total + sg * sg
    out_ref[...] = corr_ref[...] + total * (1.0 / (SEQS * SEQ_LEN))


def correction(at, g, corr, piece, prev=None, tm=512):
    kp, t = at.shape
    m = g.shape[1]
    tm = min(tm, m)
    seg = t // SEQS
    in_specs = [
        pl.BlockSpec((kp, t), lambda j: (0, 0)),
        pl.BlockSpec((t, tm), lambda j: (0, j)),
        pl.BlockSpec((kp, tm), lambda j: (piece, j)),
    ]
    args = [at, g, corr]
    aliases = {}
    if prev is not None:
        in_specs.append(pl.BlockSpec(memory_space=pl.ANY))
        args.append(prev)
        aliases = {3: 0}
    return pl.pallas_call(
        functools.partial(correction_kernel, seg),
        out_shape=jax.ShapeDtypeStruct(corr.shape, jnp.float32),
        grid=(m // tm,),
        in_specs=in_specs,
        out_specs=pl.BlockSpec((kp, tm), lambda j: (piece, j)),
        input_output_aliases=aliases,
        compiler_params=pltpu.CompilerParams(vmem_limit_bytes=48 * 1024 * 1024),
        cost_estimate=pl.CostEstimate(
            flops=2 * kp * t * m + 3 * kp * m,
            transcendentals=0,
            bytes_accessed=2 * kp * t + 2 * t * m + 8 * kp * m,
        ),
    )(*args)


def local(ring, acts, grads, basis_in, basis_out, corr):
    n_chip = lax.axis_size("rchip")
    n_row = n_chip * 2
    n_col = lax.axis_size("col")
    tok_dev = acts.shape[0]
    assert CHUNKS == 1
    half = tok_dev // CHUNKS
    tokens = tok_dev * n_row

    gathered = lax.all_gather(acts, ROW, axis=0, tiled=True)
    k_rows = basis_in.shape[0]
    kp = k_rows // K_PIECES
    parts, recvs = [], []
    for i in range(K_PIECES):
        part = lax.dot_general(
            basis_in[i * kp:(i + 1) * kp], gathered, (((1,), (1,)), ((), ())),
            preferred_element_type=jnp.float32,
        )
        parts.append(part)
        if n_col == 2:
            recvs.append(lax.ppermute(part.astype(jnp.bfloat16), "col", swap_perm(2)))

    if n_col == 2:
        other = lax.ppermute(grads, "col", swap_perm(2))
        first = lax.axis_index("col") == 0
        g_all = jnp.concatenate([jnp.where(first, grads, other), jnp.where(first, other, grads)])
    else:
        g_all = lax.all_gather(grads, "col", axis=0, tiled=True)
    per_seq = n_row // SEQS
    g_all = g_all.reshape(SEQS, per_seq, CHUNKS, half, g_all.shape[1]).transpose(0, 2, 1, 3, 4)
    g_all = g_all.reshape(tokens, grads.shape[1])
    g_part = lax.dot_general(
        g_all, basis_out, (((1,), (1,)), ((), ())), preferred_element_type=jnp.float32
    )
    core = lax.axis_index("core")
    pair = tokens // 2
    keep = lax.dynamic_slice_in_dim(g_part, core * pair, pair, axis=0)
    send = lax.dynamic_slice_in_dim(g_part, (1 - core) * pair, pair, axis=0)
    summed = keep + lax.ppermute(send, "core", swap_perm(2))
    share = ring_reduce_scatter(summed, ring, "rchip")
    grad_rot = lax.all_gather(share.astype(jnp.bfloat16), ("core", "rchip"), axis=0, tiled=True)

    out = None
    for i in range(K_PIECES):
        if n_col == 2:
            recv = recvs[i]
            if out is not None:
                out, recv = lax.optimization_barrier((out, recv))
            act_t = (parts[i] + recv.astype(jnp.float32)).astype(jnp.bfloat16)
        else:
            act_t = lax.psum(parts[i], "col").astype(jnp.bfloat16)
        out = correction(act_t, grad_rot, corr, i, out)
    return out


def solution(mesh):
    devices = np.asarray(mesh.devices)
    n_row, n_col = devices.shape
    inner = Mesh(devices.reshape(n_row // 2, 2, n_col), ("rchip", "core", "col"))
    ring = chip_ring(devices)
    return jax.shard_map(
        functools.partial(local, ring),
        mesh=inner,
        in_specs=(
            P(ROW, "col"),
            P("col", ROW),
            P(ROW, "col"),
            P("col", ROW),
            P(ROW, "col"),
        ),
        out_specs=P(ROW, "col"),
        check_vma=False,
    )
```

```python
import functools

import jax
import jax.numpy as jnp
import numpy as np
from jax import lax
from jax.experimental import pallas as pl
from jax.experimental.pallas import tpu as pltpu
from jax.sharding import Mesh
from jax.sharding import PartitionSpec as P

SEQ_LEN = 512
SEQS = 2
CHUNKS = 1
K_PIECES = 4
ROW = ("rchip", "core")


def swap_perm(n):
    return [(i, i ^ 1) for i in range(n)]


def chip_ring(devices):
    n_chip = devices.shape[0] // 2
    coords = [getattr(devices[2 * i, 0], "coords", None) for i in range(n_chip)]
    if any(c is None for c in coords):
        return list(range(n_chip))
    coords = [tuple(c) for c in coords]
    vary = [d for d in range(len(coords[0])) if len({c[d] for c in coords}) > 1]
    if len(vary) == 1:
        return sorted(range(n_chip), key=lambda i: coords[i][vary[0]])
    if len(vary) != 2:
        return list(range(n_chip))
    a, b = vary
    if len({c[a] for c in coords}) != 2:
        a, b = b, a
    if len({c[a] for c in coords}) != 2:
        return list(range(n_chip))
    lo = min(c[a] for c in coords)
    first = sorted([i for i in range(n_chip) if coords[i][a] == lo], key=lambda i: coords[i][b])
    second = sorted([i for i in range(n_chip) if coords[i][a] != lo], key=lambda i: -coords[i][b])
    return first + second


def ring_reduce_scatter(x, ring, axis):
    n = len(ring)
    blk = x.shape[0] // n
    ring_arr = jnp.asarray(ring, jnp.int32)
    pos_arr = jnp.asarray(np.argsort(ring), jnp.int32)
    p = pos_arr[lax.axis_index(axis)]
    cols = x.shape[1] // 2
    right = [(ring[i], ring[(i + 1) % n]) for i in range(n)]
    left = [(ring[i], ring[(i - 1) % n]) for i in range(n)]

    def block(part, pos):
        return lax.dynamic_slice_in_dim(part, ring_arr[pos % n] * blk, blk, axis=0)

    xa, xb = x[:, :cols], x[:, cols:]
    buf_a = block(xa, p - 1 + n)
    buf_b = block(xb, p + 1)
    for s in range(1, n):
        buf_a = lax.ppermute(buf_a, axis, right) + block(xa, p - 1 - s + 2 * n)
        buf_b = lax.ppermute(buf_b, axis, left) + block(xb, p + 1 + s)
    return jnp.concatenate([buf_a, buf_b], axis=1)


def correction_kernel(seg, at_ref, g_ref, corr_ref, *rest):
    out_ref = rest[-1]
    total = None
    for s in range(SEQS):
        cols = slice(s * seg, (s + 1) * seg)
        sg = jnp.dot(at_ref[:, cols], g_ref[cols, :], preferred_element_type=jnp.float32)
        total = sg * sg if total is None else total + sg * sg
    out_ref[...] = corr_ref[...] + total * (1.0 / (SEQS * SEQ_LEN))


def correction(at, g, corr, piece, prev=None, tm=512):
    kp, t = at.shape
    m = g.shape[1]
    tm = min(tm, m)
    seg = t // SEQS
    in_specs = [
        pl.BlockSpec((kp, t), lambda j: (0, 0)),
        pl.BlockSpec((t, tm), lambda j: (0, j)),
        pl.BlockSpec((kp, tm), lambda j: (piece, j)),
    ]
    args = [at, g, corr]
    aliases = {}
    if prev is not None:
        in_specs.append(pl.BlockSpec(memory_space=pl.ANY))
        args.append(prev)
        aliases = {3: 0}
    return pl.pallas_call(
        functools.partial(correction_kernel, seg),
        out_shape=jax.ShapeDtypeStruct(corr.shape, jnp.float32),
        grid=(m // tm,),
        in_specs=in_specs,
        out_specs=pl.BlockSpec((kp, tm), lambda j: (piece, j)),
        input_output_aliases=aliases,
        compiler_params=pltpu.CompilerParams(vmem_limit_bytes=48 * 1024 * 1024),
        cost_estimate=pl.CostEstimate(
            flops=2 * kp * t * m + 3 * kp * m,
            transcendentals=0,
            bytes_accessed=2 * kp * t + 2 * t * m + 8 * kp * m,
        ),
    )(*args)


def local(ring, acts, grads, basis_in, basis_out, corr):
    n_chip = lax.axis_size("rchip")
    n_row = n_chip * 2
    n_col = lax.axis_size("col")
    tok_dev = acts.shape[0]
    assert CHUNKS == 1
    half = tok_dev // CHUNKS
    tokens = tok_dev * n_row

    gathered = lax.all_gather(acts, ROW, axis=0, tiled=True)
    k_rows = basis_in.shape[0]
    kp = k_rows // K_PIECES
    parts, recvs = [], []
    for i in range(K_PIECES):
        part = lax.dot_general(
            basis_in[i * kp:(i + 1) * kp], gathered, (((1,), (1,)), ((), ())),
            preferred_element_type=jnp.float32,
        )
        parts.append(part)
        if n_col == 2:
            recvs.append(lax.ppermute(part.astype(jnp.bfloat16), "col", swap_perm(2)))

    if n_col == 2:
        other = lax.ppermute(grads, "col", swap_perm(2))
        first = lax.axis_index("col") == 0
        g_all = jnp.concatenate([jnp.where(first, grads, other), jnp.where(first, other, grads)])
    else:
        g_all = lax.all_gather(grads, "col", axis=0, tiled=True)
    per_seq = n_row // SEQS
    g_all = g_all.reshape(SEQS, per_seq, CHUNKS, half, g_all.shape[1]).transpose(0, 2, 1, 3, 4)
    g_all = g_all.reshape(tokens, grads.shape[1])
    g_part = lax.dot_general(
        g_all, basis_out, (((1,), (1,)), ((), ())), preferred_element_type=jnp.float32
    )
    core = lax.axis_index("core")
    pair = tokens // 2
    keep = lax.dynamic_slice_in_dim(g_part, core * pair, pair, axis=0)
    send = lax.dynamic_slice_in_dim(g_part, (1 - core) * pair, pair, axis=0)
    summed = keep + lax.ppermute(send, "core", swap_perm(2))
    share = ring_reduce_scatter(summed, ring, "rchip")
    grad_rot = lax.all_gather(share.astype(jnp.bfloat16), ("core", "rchip"), axis=0, tiled=True)

    out = None
    for i in range(K_PIECES):
        if n_col == 2:
            recv = recvs[i]
            if out is not None:
                out, recv = lax.optimization_barrier((out, recv))
            act_t = (parts[i] + recv.astype(jnp.float32)).astype(jnp.bfloat16)
        else:
            act_t = lax.psum(parts[i], "col").astype(jnp.bfloat16)
        out = correction(act_t, grad_rot, corr, i, out)
    return out


def solution(mesh):
    devices = np.asarray(mesh.devices)
    n_row, n_col = devices.shape
    inner = Mesh(devices.reshape(n_row // 2, 2, n_col), ("rchip", "core", "col"))
    ring = chip_ring(devices)
    return jax.shard_map(
        functools.partial(local, ring),
        mesh=inner,
        in_specs=(
            P(ROW, "col"),
            P("col", ROW),
            P(ROW, "col"),
            P("col", ROW),
            P(ROW, "col"),
        ),
        out_specs=P(ROW, "col"),
        check_vma=False,
    )
```

```python
import functools

import jax
import jax.numpy as jnp
import numpy as np
from jax import lax
from jax.experimental import pallas as pl
from jax.experimental.pallas import tpu as pltpu
from jax.sharding import Mesh
from jax.sharding import PartitionSpec as P

SEQ_LEN = 512
SEQS = 2
CHUNKS = 1
K_PIECES = 2
ROW = ("rchip", "core")


def swap_perm(n):
    return [(i, i ^ 1) for i in range(n)]


def chip_ring(devices):
    n_chip = devices.shape[0] // 2
    coords = [getattr(devices[2 * i, 0], "coords", None) for i in range(n_chip)]
    if any(c is None for c in coords):
        return list(range(n_chip))
    coords = [tuple(c) for c in coords]
    vary = [d for d in range(len(coords[0])) if len({c[d] for c in coords}) > 1]
    if len(vary) == 1:
        return sorted(range(n_chip), key=lambda i: coords[i][vary[0]])
    if len(vary) != 2:
        return list(range(n_chip))
    a, b = vary
    if len({c[a] for c in coords}) != 2:
        a, b = b, a
    if len({c[a] for c in coords}) != 2:
        return list(range(n_chip))
    lo = min(c[a] for c in coords)
    first = sorted([i for i in range(n_chip) if coords[i][a] == lo], key=lambda i: coords[i][b])
    second = sorted([i for i in range(n_chip) if coords[i][a] != lo], key=lambda i: -coords[i][b])
    return first + second


def ring_reduce_scatter(x, ring, axis):
    n = len(ring)
    blk = x.shape[0] // n
    ring_arr = jnp.asarray(ring, jnp.int32)
    pos_arr = jnp.asarray(np.argsort(ring), jnp.int32)
    p = pos_arr[lax.axis_index(axis)]
    cols = x.shape[1] // 2
    right = [(ring[i], ring[(i + 1) % n]) for i in range(n)]
    left = [(ring[i], ring[(i - 1) % n]) for i in range(n)]

    def block(part, pos):
        return lax.dynamic_slice_in_dim(part, ring_arr[pos % n] * blk, blk, axis=0)

    xa, xb = x[:, :cols], x[:, cols:]
    buf_a = block(xa, p - 1 + n)
    buf_b = block(xb, p + 1)
    for s in range(1, n):
        buf_a = lax.ppermute(buf_a, axis, right) + block(xa, p - 1 - s + 2 * n)
        buf_b = lax.ppermute(buf_b, axis, left) + block(xb, p + 1 + s)
    return jnp.concatenate([buf_a, buf_b], axis=1)


def correction_kernel(seg, at_ref, g_ref, corr_ref, *rest):
    out_ref = rest[-1]
    total = None
    for s in range(SEQS):
        cols = slice(s * seg, (s + 1) * seg)
        sg = jnp.dot(at_ref[:, cols], g_ref[cols, :], preferred_element_type=jnp.float32)
        total = sg * sg if total is None else total + sg * sg
    out_ref[...] = corr_ref[...] + total * (1.0 / (SEQS * SEQ_LEN))


def correction(at, g, corr, row0, tk, prev=None):
    kp, t = at.shape
    m = g.shape[1]
    seg = t // SEQS
    first = row0 // tk
    in_specs = [
        pl.BlockSpec((tk, t), lambda i: (i, 0)),
        pl.BlockSpec((t, m), lambda i: (0, 0)),
        pl.BlockSpec((tk, m), lambda i: (first + i, 0)),
    ]
    args = [at, g, corr]
    aliases = {}
    if prev is not None:
        in_specs.append(pl.BlockSpec(memory_space=pl.ANY))
        args.append(prev)
        aliases = {3: 0}
    return pl.pallas_call(
        functools.partial(correction_kernel, seg),
        out_shape=jax.ShapeDtypeStruct(corr.shape, jnp.float32),
        grid=(kp // tk,),
        in_specs=in_specs,
        out_specs=pl.BlockSpec((tk, m), lambda i: (first + i, 0)),
        input_output_aliases=aliases,
        compiler_params=pltpu.CompilerParams(vmem_limit_bytes=56 * 1024 * 1024),
        cost_estimate=pl.CostEstimate(
            flops=2 * kp * t * m + 3 * kp * m,
            transcendentals=0,
            bytes_accessed=2 * kp * t + 2 * t * m + 8 * kp * m,
        ),
    )(*args)


def local(ring, acts, grads, basis_in, basis_out, corr):
    assert K_PIECES == 2
    n_chip = lax.axis_size("rchip")
    n_row = n_chip * 2
    n_col = lax.axis_size("col")
    tok_dev = acts.shape[0]
    assert CHUNKS == 1
    half = tok_dev // CHUNKS
    tokens = tok_dev * n_row

    gathered = lax.all_gather(acts, ROW, axis=0, tiled=True)
    k_rows = basis_in.shape[0]
    tk = k_rows // 14
    bounds = [0, 9 * tk, k_rows]
    parts, recvs = [], []
    for i in range(K_PIECES):
        part = lax.dot_general(
            basis_in[bounds[i]:bounds[i + 1]], gathered, (((1,), (1,)), ((), ())),
            preferred_element_type=jnp.float32,
        )
        parts.append(part)
        if n_col == 2:
            recvs.append(lax.ppermute(part.astype(jnp.bfloat16), "col", swap_perm(2)))

    if n_col == 2:
        other = lax.ppermute(grads, "col", swap_perm(2))
        first = lax.axis_index("col") == 0
        g_all = jnp.concatenate([jnp.where(first, grads, other), jnp.where(first, other, grads)])
    else:
        g_all = lax.all_gather(grads, "col", axis=0, tiled=True)
    per_seq = n_row // SEQS
    g_all = g_all.reshape(SEQS, per_seq, CHUNKS, half, g_all.shape[1]).transpose(0, 2, 1, 3, 4)
    g_all = g_all.reshape(tokens, grads.shape[1])
    g_part = lax.dot_general(
        g_all, basis_out, (((1,), (1,)), ((), ())), preferred_element_type=jnp.float32
    )
    core = lax.axis_index("core")
    pair = tokens // 2
    keep = lax.dynamic_slice_in_dim(g_part, core * pair, pair, axis=0)
    send = lax.dynamic_slice_in_dim(g_part, (1 - core) * pair, pair, axis=0)
    summed = keep + lax.ppermute(send, "core", swap_perm(2))
    share = ring_reduce_scatter(summed, ring, "rchip")
    grad_rot = lax.all_gather(share.astype(jnp.bfloat16), ("core", "rchip"), axis=0, tiled=True)

    out = None
    for i in range(K_PIECES):
        if n_col == 2:
            recv = recvs[i]
            if out is not None:
                out, recv = lax.optimization_barrier((out, recv))
            act_t = (parts[i] + recv.astype(jnp.float32)).astype(jnp.bfloat16)
        else:
            act_t = lax.psum(parts[i], "col").astype(jnp.bfloat16)
        out = correction(act_t, grad_rot, corr, bounds[i], tk, out)
    return out


def solution(mesh):
    devices = np.asarray(mesh.devices)
    n_row, n_col = devices.shape
    inner = Mesh(devices.reshape(n_row // 2, 2, n_col), ("rchip", "core", "col"))
    ring = chip_ring(devices)
    return jax.shard_map(
        functools.partial(local, ring),
        mesh=inner,
        in_specs=(
            P(ROW, "col"),
            P("col", ROW),
            P(ROW, "col"),
            P("col", ROW),
            P(ROW, "col"),
        ),
        out_specs=P(ROW, "col"),
        check_vma=False,
    )
```

```python
import functools

import jax
import jax.numpy as jnp
import numpy as np
from jax import lax
from jax.experimental import pallas as pl
from jax.experimental.pallas import tpu as pltpu
from jax.sharding import Mesh
from jax.sharding import PartitionSpec as P

SEQ_LEN = 512
SEQS = 2
CHUNKS = 1
K_PIECES = 2
ROW = ("rchip", "core")


def swap_perm(n):
    return [(i, i ^ 1) for i in range(n)]


def chip_ring(devices):
    n_chip = devices.shape[0] // 2
    coords = [getattr(devices[2 * i, 0], "coords", None) for i in range(n_chip)]
    if any(c is None for c in coords):
        return list(range(n_chip))
    coords = [tuple(c) for c in coords]
    vary = [d for d in range(len(coords[0])) if len({c[d] for c in coords}) > 1]
    if len(vary) == 1:
        return sorted(range(n_chip), key=lambda i: coords[i][vary[0]])
    if len(vary) != 2:
        return list(range(n_chip))
    a, b = vary
    if len({c[a] for c in coords}) != 2:
        a, b = b, a
    if len({c[a] for c in coords}) != 2:
        return list(range(n_chip))
    lo = min(c[a] for c in coords)
    first = sorted([i for i in range(n_chip) if coords[i][a] == lo], key=lambda i: coords[i][b])
    second = sorted([i for i in range(n_chip) if coords[i][a] != lo], key=lambda i: -coords[i][b])
    return first + second


def ring_reduce_scatter(x, ring, axis):
    n = len(ring)
    blk = x.shape[0] // n
    ring_arr = jnp.asarray(ring, jnp.int32)
    pos_arr = jnp.asarray(np.argsort(ring), jnp.int32)
    p = pos_arr[lax.axis_index(axis)]
    cols = x.shape[1] // 2
    right = [(ring[i], ring[(i + 1) % n]) for i in range(n)]
    left = [(ring[i], ring[(i - 1) % n]) for i in range(n)]

    def block(part, pos):
        return lax.dynamic_slice_in_dim(part, ring_arr[pos % n] * blk, blk, axis=0)

    xa, xb = x[:, :cols], x[:, cols:]
    buf_a = block(xa, p - 1 + n)
    buf_b = block(xb, p + 1)
    for s in range(1, n):
        buf_a = lax.ppermute(buf_a, axis, right) + block(xa, p - 1 - s + 2 * n)
        buf_b = lax.ppermute(buf_b, axis, left) + block(xb, p + 1 + s)
    return jnp.concatenate([buf_a, buf_b], axis=1)


def correction_kernel(seg, at_ref, g_ref, corr_ref, *rest):
    out_ref = rest[-1]
    total = None
    for s in range(SEQS):
        cols = slice(s * seg, (s + 1) * seg)
        sg = jnp.dot(at_ref[:, cols], g_ref[cols, :], preferred_element_type=jnp.float32)
        total = sg * sg if total is None else total + sg * sg
    out_ref[...] = corr_ref[...] + total * (1.0 / (SEQS * SEQ_LEN))


def correction(at, g, corr, piece, prev=None, tm=1024):
    kp, t = at.shape
    m = g.shape[1]
    tm = min(tm, m)
    seg = t // SEQS
    in_specs = [
        pl.BlockSpec((kp, t), lambda j: (0, 0)),
        pl.BlockSpec((t, tm), lambda j: (0, j)),
        pl.BlockSpec((kp, tm), lambda j: (piece, j)),
    ]
    args = [at, g, corr]
    aliases = {}
    if prev is not None:
        in_specs.append(pl.BlockSpec(memory_space=pl.ANY))
        args.append(prev)
        aliases = {3: 0}
    return pl.pallas_call(
        functools.partial(correction_kernel, seg),
        out_shape=jax.ShapeDtypeStruct(corr.shape, jnp.float32),
        grid=(m // tm,),
        in_specs=in_specs,
        out_specs=pl.BlockSpec((kp, tm), lambda j: (piece, j)),
        input_output_aliases=aliases,
        compiler_params=pltpu.CompilerParams(vmem_limit_bytes=48 * 1024 * 1024),
        cost_estimate=pl.CostEstimate(
            flops=2 * kp * t * m + 3 * kp * m,
            transcendentals=0,
            bytes_accessed=2 * kp * t + 2 * t * m + 8 * kp * m,
        ),
    )(*args)


def local(ring, acts, grads, basis_in, basis_out, corr):
    n_chip = lax.axis_size("rchip")
    n_row = n_chip * 2
    n_col = lax.axis_size("col")
    tok_dev = acts.shape[0]
    assert CHUNKS == 1
    half = tok_dev // CHUNKS
    tokens = tok_dev * n_row

    gathered = lax.all_gather(acts, ROW, axis=0, tiled=True)
    k_rows = basis_in.shape[0]
    kp = k_rows // K_PIECES
    parts, recvs = [], []
    for i in range(K_PIECES):
        part = lax.dot_general(
            basis_in[i * kp:(i + 1) * kp], gathered, (((1,), (1,)), ((), ())),
            preferred_element_type=jnp.float32,
        )
        parts.append(part)
        if n_col == 2:
            recvs.append(lax.ppermute(part.astype(jnp.bfloat16), "col", swap_perm(2)))

    if n_col == 2:
        other = lax.ppermute(grads, "col", swap_perm(2))
        first = lax.axis_index("col") == 0
        g_all = jnp.concatenate([jnp.where(first, grads, other), jnp.where(first, other, grads)])
    else:
        g_all = lax.all_gather(grads, "col", axis=0, tiled=True)
    per_seq = n_row // SEQS
    g_all = g_all.reshape(SEQS, per_seq, CHUNKS, half, g_all.shape[1]).transpose(0, 2, 1, 3, 4)
    g_all = g_all.reshape(tokens, grads.shape[1])
    g_part = lax.dot_general(
        g_all, basis_out, (((1,), (1,)), ((), ())), preferred_element_type=jnp.float32
    )
    core = lax.axis_index("core")
    pair = tokens // 2
    keep = lax.dynamic_slice_in_dim(g_part, core * pair, pair, axis=0)
    send = lax.dynamic_slice_in_dim(g_part, (1 - core) * pair, pair, axis=0)
    summed = keep + lax.ppermute(send, "core", swap_perm(2))
    share = ring_reduce_scatter(summed, ring, "rchip")
    grad_rot = lax.all_gather(share.astype(jnp.bfloat16), ("core", "rchip"), axis=0, tiled=True)

    out = None
    for i in range(K_PIECES):
        if n_col == 2:
            recv = recvs[i]
            if out is not None:
                out, recv = lax.optimization_barrier((out, recv))
            act_t = (parts[i] + recv.astype(jnp.float32)).astype(jnp.bfloat16)
        else:
            act_t = lax.psum(parts[i], "col").astype(jnp.bfloat16)
        out = correction(act_t, grad_rot, corr, i, out)
    return out


def solution(mesh):
    devices = np.asarray(mesh.devices)
    n_row, n_col = devices.shape
    inner = Mesh(devices.reshape(n_row // 2, 2, n_col), ("rchip", "core", "col"))
    ring = chip_ring(devices)
    return jax.shard_map(
        functools.partial(local, ring),
        mesh=inner,
        in_specs=(
            P(ROW, "col"),
            P("col", ROW),
            P(ROW, "col"),
            P("col", ROW),
            P(ROW, "col"),
        ),
        out_specs=P(ROW, "col"),
        check_vma=False,
    )
```

```python
import functools

import jax
import jax.numpy as jnp
import numpy as np
from jax import lax
from jax.experimental import pallas as pl
from jax.experimental.pallas import tpu as pltpu
from jax.sharding import Mesh
from jax.sharding import PartitionSpec as P

SEQ_LEN = 512
SEQS = 2
CHUNKS = 1
K_PIECES = 2
ROW = ("rchip", "core")


def swap_perm(n):
    return [(i, i ^ 1) for i in range(n)]


def chip_ring(devices):
    n_chip = devices.shape[0] // 2
    coords = [getattr(devices[2 * i, 0], "coords", None) for i in range(n_chip)]
    if any(c is None for c in coords):
        return list(range(n_chip))
    coords = [tuple(c) for c in coords]
    vary = [d for d in range(len(coords[0])) if len({c[d] for c in coords}) > 1]
    if len(vary) == 1:
        return sorted(range(n_chip), key=lambda i: coords[i][vary[0]])
    if len(vary) != 2:
        return list(range(n_chip))
    a, b = vary
    if len({c[a] for c in coords}) != 2:
        a, b = b, a
    if len({c[a] for c in coords}) != 2:
        return list(range(n_chip))
    lo = min(c[a] for c in coords)
    first = sorted([i for i in range(n_chip) if coords[i][a] == lo], key=lambda i: coords[i][b])
    second = sorted([i for i in range(n_chip) if coords[i][a] != lo], key=lambda i: -coords[i][b])
    return first + second


def ring_reduce_scatter(x, ring, axis):
    n = len(ring)
    blk = x.shape[0] // n
    ring_arr = jnp.asarray(ring, jnp.int32)
    pos_arr = jnp.asarray(np.argsort(ring), jnp.int32)
    p = pos_arr[lax.axis_index(axis)]
    cols = x.shape[1] // 2
    right = [(ring[i], ring[(i + 1) % n]) for i in range(n)]
    left = [(ring[i], ring[(i - 1) % n]) for i in range(n)]

    def block(part, pos):
        return lax.dynamic_slice_in_dim(part, ring_arr[pos % n] * blk, blk, axis=0)

    xa, xb = x[:, :cols], x[:, cols:]
    buf_a = block(xa, p - 1 + n)
    buf_b = block(xb, p + 1)
    for s in range(1, n):
        buf_a = lax.ppermute(buf_a, axis, right) + block(xa, p - 1 - s + 2 * n)
        buf_b = lax.ppermute(buf_b, axis, left) + block(xb, p + 1 + s)
    return jnp.concatenate([buf_a, buf_b], axis=1)


def correction_kernel(seg, at_ref, g_ref, corr_ref, *rest):
    out_ref = rest[-1]
    total = None
    for s in range(SEQS):
        cols = slice(s * seg, (s + 1) * seg)
        sg = jnp.dot(at_ref[:, cols], g_ref[cols, :], preferred_element_type=jnp.float32)
        total = sg * sg if total is None else total + sg * sg
    out_ref[...] = corr_ref[...] + total * (1.0 / (SEQS * SEQ_LEN))


def correction(at, g, corr, piece, prev=None, tm=1024):
    kp, t = at.shape
    m = g.shape[1]
    tm = min(tm, m)
    seg = t // SEQS
    in_specs = [
        pl.BlockSpec((kp, t), lambda j: (0, 0)),
        pl.BlockSpec((t, tm), lambda j: (0, j)),
        pl.BlockSpec((kp, tm), lambda j: (piece, j)),
    ]
    args = [at, g, corr]
    aliases = {}
    if prev is not None:
        in_specs.append(pl.BlockSpec(memory_space=pl.ANY))
        args.append(prev)
        aliases = {3: 0}
    return pl.pallas_call(
        functools.partial(correction_kernel, seg),
        out_shape=jax.ShapeDtypeStruct(corr.shape, jnp.float32),
        grid=(m // tm,),
        in_specs=in_specs,
        out_specs=pl.BlockSpec((kp, tm), lambda j: (piece, j)),
        input_output_aliases=aliases,
        compiler_params=pltpu.CompilerParams(vmem_limit_bytes=48 * 1024 * 1024),
        cost_estimate=pl.CostEstimate(
            flops=2 * kp * t * m + 3 * kp * m,
            transcendentals=0,
            bytes_accessed=2 * kp * t + 2 * t * m + 8 * kp * m,
        ),
    )(*args)


def local(ring, acts, grads, basis_in, basis_out, corr):
    n_chip = lax.axis_size("rchip")
    n_row = n_chip * 2
    n_col = lax.axis_size("col")
    tok_dev = acts.shape[0]
    assert CHUNKS == 1
    half = tok_dev // CHUNKS
    tokens = tok_dev * n_row

    gathered = lax.all_gather(acts, ROW, axis=0, tiled=True)
    k_rows = basis_in.shape[0]
    kp = k_rows // K_PIECES
    parts, recvs = [], []
    for i in range(K_PIECES):
        part = lax.dot_general(
            basis_in[i * kp:(i + 1) * kp], gathered, (((1,), (1,)), ((), ())),
            preferred_element_type=jnp.float32,
        )
        parts.append(part)
        if n_col == 2:
            recvs.append(lax.ppermute(part.astype(jnp.bfloat16), "col", swap_perm(2)))

    if n_col == 2:
        other = lax.ppermute(grads, "col", swap_perm(2))
        first = lax.axis_index("col") == 0
        g_all = jnp.concatenate([jnp.where(first, grads, other), jnp.where(first, other, grads)])
    else:
        g_all = lax.all_gather(grads, "col", axis=0, tiled=True)
    per_seq = n_row // SEQS
    g_all = g_all.reshape(SEQS, per_seq, CHUNKS, half, g_all.shape[1]).transpose(0, 2, 1, 3, 4)
    g_all = g_all.reshape(tokens, grads.shape[1])
    core = lax.axis_index("core")
    pair = tokens // 2
    dims = (((1,), (1,)), ((), ()))
    send_rows = lax.dynamic_slice_in_dim(g_all, (1 - core) * pair, pair, axis=0)
    send = lax.dot_general(send_rows, basis_out, dims, preferred_element_type=jnp.float32)
    received = lax.ppermute(send, "core", swap_perm(2))
    keep_rows = lax.dynamic_slice_in_dim(g_all, core * pair, pair, axis=0)
    keep = lax.dot_general(keep_rows, basis_out, dims, preferred_element_type=jnp.float32)
    summed = keep + received
    share = ring_reduce_scatter(summed, ring, "rchip")
    grad_rot = lax.all_gather(share.astype(jnp.bfloat16), ("core", "rchip"), axis=0, tiled=True)

    out = None
    for i in range(K_PIECES):
        if n_col == 2:
            recv = recvs[i]
            if out is not None:
                out, recv = lax.optimization_barrier((out, recv))
            act_t = (parts[i] + recv.astype(jnp.float32)).astype(jnp.bfloat16)
        else:
            act_t = lax.psum(parts[i], "col").astype(jnp.bfloat16)
        out = correction(act_t, grad_rot, corr, i, out)
    return out


def solution(mesh):
    devices = np.asarray(mesh.devices)
    n_row, n_col = devices.shape
    inner = Mesh(devices.reshape(n_row // 2, 2, n_col), ("rchip", "core", "col"))
    ring = chip_ring(devices)
    return jax.shard_map(
        functools.partial(local, ring),
        mesh=inner,
        in_specs=(
            P(ROW, "col"),
            P("col", ROW),
            P(ROW, "col"),
            P("col", ROW),
            P(ROW, "col"),
        ),
        out_specs=P(ROW, "col"),
        check_vma=False,
    )
```

```python
import functools

import jax
import jax.numpy as jnp
import numpy as np
from jax import lax
from jax.experimental import pallas as pl
from jax.experimental.pallas import tpu as pltpu
from jax.sharding import Mesh
from jax.sharding import PartitionSpec as P

SEQ_LEN = 512
SEQS = 2
CHUNKS = 1
K_PIECES = 2
ROW = ("rchip", "core")


def swap_perm(n):
    return [(i, i ^ 1) for i in range(n)]


def chip_ring(devices):
    n_chip = devices.shape[0] // 2
    coords = [getattr(devices[2 * i, 0], "coords", None) for i in range(n_chip)]
    if any(c is None for c in coords):
        return list(range(n_chip))
    coords = [tuple(c) for c in coords]
    vary = [d for d in range(len(coords[0])) if len({c[d] for c in coords}) > 1]
    if len(vary) == 1:
        return sorted(range(n_chip), key=lambda i: coords[i][vary[0]])
    if len(vary) != 2:
        return list(range(n_chip))
    a, b = vary
    if len({c[a] for c in coords}) != 2:
        a, b = b, a
    if len({c[a] for c in coords}) != 2:
        return list(range(n_chip))
    lo = min(c[a] for c in coords)
    first = sorted([i for i in range(n_chip) if coords[i][a] == lo], key=lambda i: coords[i][b])
    second = sorted([i for i in range(n_chip) if coords[i][a] != lo], key=lambda i: -coords[i][b])
    return first + second


def ring_reduce_scatter(x, ring, axis):
    n = len(ring)
    blk = x.shape[0] // n
    ring_arr = jnp.asarray(ring, jnp.int32)
    pos_arr = jnp.asarray(np.argsort(ring), jnp.int32)
    p = pos_arr[lax.axis_index(axis)]
    cols = x.shape[1] // 2
    right = [(ring[i], ring[(i + 1) % n]) for i in range(n)]
    left = [(ring[i], ring[(i - 1) % n]) for i in range(n)]

    def block(part, pos):
        return lax.dynamic_slice_in_dim(part, ring_arr[pos % n] * blk, blk, axis=0)

    xa, xb = x[:, :cols], x[:, cols:]
    buf_a = block(xa, p - 1 + n)
    buf_b = block(xb, p + 1)
    for s in range(1, n):
        buf_a = lax.ppermute(buf_a, axis, right) + block(xa, p - 1 - s + 2 * n)
        buf_b = lax.ppermute(buf_b, axis, left) + block(xb, p + 1 + s)
    return jnp.concatenate([buf_a, buf_b], axis=1)


def correction_kernel(seg, part_ref, recv_ref, g_ref, corr_ref, *rest):
    out_ref, at_ref = rest[-2], rest[-1]

    @pl.when(pl.program_id(0) == 0)
    def _():
        at_ref[...] = (part_ref[...] + recv_ref[...].astype(jnp.float32)).astype(jnp.bfloat16)

    total = None
    for s in range(SEQS):
        cols = slice(s * seg, (s + 1) * seg)
        sg = jnp.dot(at_ref[:, cols], g_ref[cols, :], preferred_element_type=jnp.float32)
        total = sg * sg if total is None else total + sg * sg
    out_ref[...] = corr_ref[...] + total * (1.0 / (SEQS * SEQ_LEN))


def correction(part, recv, g, corr, piece, prev=None, tm=1024):
    kp, t = part.shape
    m = g.shape[1]
    tm = min(tm, m)
    seg = t // SEQS
    in_specs = [
        pl.BlockSpec((kp, t), lambda j: (0, 0)),
        pl.BlockSpec((kp, t), lambda j: (0, 0)),
        pl.BlockSpec((t, tm), lambda j: (0, j)),
        pl.BlockSpec((kp, tm), lambda j: (piece, j)),
    ]
    args = [part, recv, g, corr]
    aliases = {}
    if prev is not None:
        in_specs.append(pl.BlockSpec(memory_space=pl.ANY))
        args.append(prev)
        aliases = {4: 0}
    return pl.pallas_call(
        functools.partial(correction_kernel, seg),
        out_shape=jax.ShapeDtypeStruct(corr.shape, jnp.float32),
        grid=(m // tm,),
        in_specs=in_specs,
        out_specs=pl.BlockSpec((kp, tm), lambda j: (piece, j)),
        scratch_shapes=[pltpu.VMEM((kp, t), jnp.bfloat16)],
        input_output_aliases=aliases,
        compiler_params=pltpu.CompilerParams(
            vmem_limit_bytes=56 * 1024 * 1024, dimension_semantics=("arbitrary",)
        ),
        cost_estimate=pl.CostEstimate(
            flops=2 * kp * t * m + 3 * kp * m,
            transcendentals=0,
            bytes_accessed=6 * kp * t + 2 * t * m + 8 * kp * m,
        ),
    )(*args)


def local(ring, acts, grads, basis_in, basis_out, corr):
    n_chip = lax.axis_size("rchip")
    n_row = n_chip * 2
    n_col = lax.axis_size("col")
    tok_dev = acts.shape[0]
    assert CHUNKS == 1
    half = tok_dev // CHUNKS
    tokens = tok_dev * n_row

    gathered = lax.all_gather(acts, ROW, axis=0, tiled=True)
    k_rows = basis_in.shape[0]
    kp = k_rows // K_PIECES
    parts, recvs = [], []
    for i in range(K_PIECES):
        part = lax.dot_general(
            basis_in[i * kp:(i + 1) * kp], gathered, (((1,), (1,)), ((), ())),
            preferred_element_type=jnp.float32,
        )
        parts.append(part)
        if n_col == 2:
            recvs.append(lax.ppermute(part.astype(jnp.bfloat16), "col", swap_perm(2)))

    if n_col == 2:
        other = lax.ppermute(grads, "col", swap_perm(2))
        first = lax.axis_index("col") == 0
        g_all = jnp.concatenate([jnp.where(first, grads, other), jnp.where(first, other, grads)])
    else:
        g_all = lax.all_gather(grads, "col", axis=0, tiled=True)
    per_seq = n_row // SEQS
    g_all = g_all.reshape(SEQS, per_seq, CHUNKS, half, g_all.shape[1]).transpose(0, 2, 1, 3, 4)
    g_all = g_all.reshape(tokens, grads.shape[1])
    core = lax.axis_index("core")
    pair = tokens // 2
    dims = (((1,), (1,)), ((), ()))
    send_rows = lax.dynamic_slice_in_dim(g_all, (1 - core) * pair, pair, axis=0)
    send = lax.dot_general(send_rows, basis_out, dims, preferred_element_type=jnp.float32)
    received = lax.ppermute(send, "core", swap_perm(2))
    keep_rows = lax.dynamic_slice_in_dim(g_all, core * pair, pair, axis=0)
    keep = lax.dot_general(keep_rows, basis_out, dims, preferred_element_type=jnp.float32)
    summed = keep + received
    share = ring_reduce_scatter(summed, ring, "rchip")
    grad_rot = lax.all_gather(share.astype(jnp.bfloat16), ("core", "rchip"), axis=0, tiled=True)

    out = None
    for i in range(K_PIECES):
        if n_col == 2:
            recv = recvs[i]
            if out is not None:
                out, recv = lax.optimization_barrier((out, recv))
            part = parts[i]
        else:
            part = lax.psum(parts[i], "col")
            recv = jnp.zeros(part.shape, jnp.bfloat16)
        out = correction(part, recv, grad_rot, corr, i, out)
    return out


def solution(mesh):
    devices = np.asarray(mesh.devices)
    n_row, n_col = devices.shape
    inner = Mesh(devices.reshape(n_row // 2, 2, n_col), ("rchip", "core", "col"))
    ring = chip_ring(devices)
    return jax.shard_map(
        functools.partial(local, ring),
        mesh=inner,
        in_specs=(
            P(ROW, "col"),
            P("col", ROW),
            P(ROW, "col"),
            P("col", ROW),
            P(ROW, "col"),
        ),
        out_specs=P(ROW, "col"),
        check_vma=False,
    )
```
